256 devices in a mesh: cp: 64 (over z, x, y_hi), dp: 4 (over y_lo, core).
Axes of the slice: x: 4, y: 4 (y_hi: 2, y_lo: 2; y = y_hi * 2 + y_lo), z: 8, core: 2. Of those that a mesh axis runs over, the one named last changes fastest.
Arguments:
- queries: bfloat16 [4, 8192, 2560], P('dp', 'cp'), may hold values from -6 to 6
- keys: bfloat16 [4, 8192, 2560], P('dp', 'cp'), may hold values from -6 to 6
- values: bfloat16 [4, 8192, 2560], P('dp', 'cp'), may hold values from -6 to 6
- outputs: bfloat16 [4, 8192, 2560], P('dp', 'cp'), may hold values from -6 to 6
- d_out: bfloat16 [4, 8192, 2560], P('dp', 'cp'), may hold values from -6 to 6
- log_norm: float32 [4, 8192, 20], P('dp', 'cp'), may hold values from 3 to 7
- lengths: int32 [4, 17], P('dp'), may hold values from 1 to 4, as said below
- fire_w1: float32 [32], replicated, may hold values from -6 to 6
- fire_b1: float32 [32], replicated, may hold values from -3 to 3
- fire_w2: float32 [32, 20], replicated, may hold values from -1 to 1
Outputs:
- grad_queries: bfloat16 [4, 8192, 2560], P('dp', 'cp')
- grad_keys: bfloat16 [4, 8192, 2560], P('dp', 'cp')
- grad_values: bfloat16 [4, 8192, 2560], P('dp', 'cp')
- grad_w1: float32 [32], replicated
- grad_b1: float32 [32], replicated
- grad_w2: float32 [32, 20], replicated
The draws below stay inside these ranges and needn't reach their ends.
Inputs may be any that keep to these rules, and one draw needn't show every extreme that they name: `lengths`: each batch row's 17 sequences fill its 64 blocks in order, each a whole number of blocks; the first sequence of every row takes exactly 4 blocks.
All inputs are finite; a program needn't handle non-finite values.
Results may differ from the reference program's by a relative error of at most 0.0054.
Values may be sent and summed in bfloat16 or wider, within the bound.
No kernel may reach another device: no remote copies, remote signals or barrier semaphores. Data moves between devices by JAX's collectives and lax.ppermute only.
A program may use at most 128 MiB of HBM per device.

```python
import jax
import jax.numpy as jnp
from jax import lax

HEADS = 20
HEAD_DIM = 128
FIRE_HID = 32
TOK_DEV = 128
GROUP_MOST = 4
WIDTH = 2560
TOKENS = 8192
NSEQ = 17
N_CP = 64
N_DP = 4


def draw_lengths(key, part):
    slots = NSEQ - 1
    spare = GROUP_MOST - 1
    units = slots * spare
    extra = N_CP - GROUP_MOST - slots
    row_keys = jax.random.split(jax.random.fold_in(key, 17), N_DP)

    def one_row(row_key):
        order = jax.random.permutation(row_key, units)
        chosen = (order < extra).astype(jnp.int32)
        owner = jnp.arange(units, dtype=jnp.int32) // spare
        counts = jnp.sum((owner[None, :] == jnp.arange(slots, dtype=jnp.int32)[:, None]).astype(jnp.int32) * chosen[None, :], axis=1)
        return jnp.concatenate([jnp.full((1,), GROUP_MOST, jnp.int32), (1 + counts).astype(jnp.int32)])
    return jax.vmap(one_row)(row_keys).astype(jnp.int32)


def block_scale(rng, extent, cuts, least, top_value):
    level, own = 1.0, jax.random.fold_in(rng, 6)
    for position, parts in cuts:
        steps = jnp.exp(jax.random.uniform(jax.random.fold_in(own, position), (parts,), jnp.float32, least / len(cuts), top_value / len(cuts)))
        level = level * jnp.repeat(steps, extent[position] // parts).reshape([-1 if axis == position else 1 for axis in range(len(extent))])
    return level


def normal_values(own_key, dims, width, limit, cuts=(), held_as=jnp.bfloat16):
    loudness = block_scale(own_key, dims, cuts, -0.22, 0.18) if cuts else 1.0
    values = jax.random.normal(own_key, dims, jnp.float32) * width * loudness
    return jnp.minimum(jnp.maximum(values, -limit), limit).astype(held_as)


def setup_inputs(seed: int = 0) -> dict:
    key_list = jax.random.split(jax.random.key(seed), 11)
    queries = normal_values(key_list[0], (N_DP, TOKENS, WIDTH), 1.0, 6.0, ((0, 4), (1, 64)))
    keys = normal_values(key_list[1], (N_DP, TOKENS, WIDTH), 1.0, 6.0, ((0, 4), (1, 64)))
    values = normal_values(key_list[2], (N_DP, TOKENS, WIDTH), 1.0, 6.0, ((0, 4), (1, 64)))
    outputs = normal_values(key_list[3], (N_DP, TOKENS, WIDTH), 1.0, 6.0, ((0, 4), (1, 64)))
    d_out = normal_values(key_list[4], (N_DP, TOKENS, WIDTH), 1.0, 6.0, ((0, 4), (1, 64)))
    log_norm = jnp.clip(3.0 + 4.0 * jax.random.uniform(key_list[5], (N_DP, TOKENS, HEADS), jnp.float32) ** block_scale(key_list[5], (N_DP, TOKENS, HEADS), ((0, 4), (1, 64)), -0.2, 0.2), 3.0, 7.0)
    lengths = draw_lengths(jax.random.fold_in(key_list[10], 71), 0)
    fire_w1 = normal_values(key_list[7], (FIRE_HID,), 2.0, 6.0, (), jnp.float32)
    fire_b1 = normal_values(key_list[8], (FIRE_HID,), 0.5, 3.0, (), jnp.float32)
    fire_w2 = normal_values(key_list[9], (FIRE_HID, HEADS), FIRE_HID ** -0.5, 1.0, (), jnp.float32)
    return {"queries": queries, "keys": keys, "values": values, "outputs": outputs, "d_out": d_out, "log_norm": log_norm, "lengths": lengths, "fire_w1": fire_w1, "fire_b1": fire_b1, "fire_w2": fire_w2}


fire_floor = 64.0


def seat_of(length_row, device):
    ends = jnp.cumsum(length_row)
    sequence = jnp.sum((ends <= device).astype(jnp.int32))
    before = jnp.sum(jnp.where(jnp.arange(length_row.shape[0], dtype=jnp.int32) < sequence, length_row, 0))
    return sequence, device - before


def pair_terms(query_heads, grad_heads, log_block, delta_block, key_heads, value_heads, query_seq, query_pos, key_seq, key_pos, fire_w1, fire_b1, fire_w2):
    highest = lax.Precision.HIGHEST
    scale_value = query_heads.shape[2] ** -0.5
    allowed = (query_seq == key_seq) & (key_pos[None, :] <= query_pos[:, None])
    distance = jnp.maximum(query_pos[:, None] - key_pos[None, :], 0).astype(jnp.float32)
    denom = jnp.log1p(jnp.maximum(query_pos.astype(jnp.float32), fire_floor))
    ratio = jnp.log1p(distance) / denom[:, None]
    hidden_pre = fire_w1[:, None, None] * ratio[None] + fire_b1[:, None, None]
    hidden_act = jnp.maximum(hidden_pre, 0.0)
    pair_bias = jnp.einsum("cqk,ch->hqk", hidden_act, fire_w2, precision=highest)
    query_f = query_heads.astype(jnp.float32)
    key_f = key_heads.astype(jnp.float32)
    value_f = value_heads.astype(jnp.float32)
    grad_f = grad_heads.astype(jnp.float32)
    scores = jnp.einsum("qhd,khd->hqk", query_f, key_f) * scale_value + pair_bias
    shifted = jnp.where(allowed[None], scores - log_block.T[:, :, None], -1e30)
    prob_block = jnp.exp(shifted)
    dprob = jnp.einsum("qhd,khd->hqk", grad_f, value_f)
    dscore = prob_block * (dprob - delta_block.T[:, :, None])
    prob_low = lax.optimization_barrier(prob_block.astype(jnp.bfloat16)).astype(jnp.float32)
    score_low = lax.optimization_barrier(dscore.astype(jnp.bfloat16)).astype(jnp.float32)
    grad_query = jnp.einsum("hqk,khd->qhd", score_low, key_f) * scale_value
    grad_key = jnp.einsum("hqk,qhd->khd", score_low, query_f) * scale_value
    grad_value = jnp.einsum("hqk,qhd->khd", prob_low, grad_f)
    grad_second = jnp.einsum("hqk,cqk->ch", dscore, hidden_act, precision=highest)
    grad_act = jnp.einsum("hqk,ch->cqk", dscore, fire_w2, precision=highest)
    grad_pre = jnp.where(hidden_pre > 0, grad_act, 0.0)
    grad_first = jnp.sum(grad_pre * ratio[None], axis=(1, 2))
    grad_bias = jnp.sum(grad_pre, axis=(1, 2))
    return grad_query, grad_key, grad_value, grad_first, grad_bias, grad_second


def reference(queries, keys, values, outputs, d_out, log_norm, lengths, fire_w1, fire_b1, fire_w2):
    block_shape = (N_CP, TOK_DEV, HEADS, HEAD_DIM)
    total_first = jnp.zeros((FIRE_HID,), jnp.float32)
    total_bias = jnp.zeros((FIRE_HID,), jnp.float32)
    total_second = jnp.zeros((FIRE_HID, HEADS), jnp.float32)
    all_q, all_k, all_v = [], [], []
    for batch_row in range(N_DP):
        query_blocks = queries[batch_row].reshape(block_shape)
        key_blocks = keys[batch_row].reshape(block_shape)
        value_blocks = values[batch_row].reshape(block_shape)
        grad_blocks = d_out[batch_row].reshape(block_shape)
        out_blocks = outputs[batch_row].reshape(block_shape)
        log_blocks = log_norm[batch_row].reshape(N_CP, TOK_DEV, HEADS)
        delta_blocks = jnp.einsum("nqhd,nqhd->nqh", grad_blocks.astype(jnp.float32), out_blocks.astype(jnp.float32))
        length_row = lengths[batch_row]
        seq_ids, offsets = jax.vmap(lambda device: seat_of(length_row, device))(jnp.arange(N_CP, dtype=jnp.int32))
        positions = offsets[:, None] * TOK_DEV + jnp.arange(TOK_DEV, dtype=jnp.int32)[None, :]
        sum_q = jnp.zeros(block_shape, jnp.float32)
        sum_k = jnp.zeros(block_shape, jnp.float32)
        sum_v = jnp.zeros(block_shape, jnp.float32)
        for hop_index in range(GROUP_MOST):
            def one_block(index, hop=hop_index):
                key_index = (index - hop) % N_CP

                def live(unused):
                    return pair_terms(query_blocks[index], grad_blocks[index], log_blocks[index], delta_blocks[index], key_blocks[key_index], value_blocks[key_index], seq_ids[index], positions[index], seq_ids[key_index], positions[key_index], fire_w1, fire_b1, fire_w2)

                def dead(unused):
                    zero_block = jnp.zeros((TOK_DEV, HEADS, HEAD_DIM), jnp.float32)
                    return (zero_block, zero_block, zero_block, jnp.zeros((FIRE_HID,), jnp.float32), jnp.zeros((FIRE_HID,), jnp.float32), jnp.zeros((FIRE_HID, HEADS), jnp.float32))

                return lax.cond(seq_ids[index] == seq_ids[key_index], live, dead, 0)

            result = lax.map(one_block, jnp.arange(N_CP, dtype=jnp.int32))
            sum_q = sum_q + result[0]
            sum_k = sum_k + jnp.roll(result[1], -hop_index, axis=0)
            sum_v = sum_v + jnp.roll(result[2], -hop_index, axis=0)
            total_first = total_first + jnp.sum(result[3], axis=0)
            total_bias = total_bias + jnp.sum(result[4], axis=0)
            total_second = total_second + jnp.sum(result[5], axis=0)
        all_q.append(sum_q.reshape(TOKENS, WIDTH).astype(jnp.bfloat16))
        all_k.append(sum_k.reshape(TOKENS, WIDTH).astype(jnp.bfloat16))
        all_v.append(sum_v.reshape(TOKENS, WIDTH).astype(jnp.bfloat16))
    factor = (N_DP * TOKENS) ** -0.5
    return (jnp.stack(all_q), jnp.stack(all_k), jnp.stack(all_v), total_first * factor, total_bias * factor, total_second * factor)
```

```python
import jax
import jax.numpy as jnp
from jax import lax
from jax.sharding import PartitionSpec as P

GROUP_MOST = 4


fire_floor = 64.0


def shifted_2(block, axis, distance):
    devices = range(lax.axis_size(axis))
    route = [(i - distance, i) for i in devices if i - distance in devices]
    return lax.ppermute(block, axis, route)


def shifted_3(shard, axis, by):
    count = lax.axis_size(axis)
    return lax.ppermute(shard, axis, [(i, (i + by) % count) for i in range(count)])


def seat_of(length_row, device):
    ends = jnp.cumsum(length_row)
    sequence = jnp.sum((ends <= device).astype(jnp.int32))
    before = jnp.sum(
        jnp.where(jnp.arange(length_row.shape[0], dtype=jnp.int32) < sequence, length_row, 0)
    )
    return (sequence, device - before)


def pair_terms(
    query_heads,
    grad_heads,
    log_block,
    delta_block,
    key_heads,
    value_heads,
    query_seq,
    query_pos,
    key_seq,
    key_pos,
    fire_w1,
    fire_b1,
    fire_w2,
):
    highest = lax.Precision.HIGHEST
    scale_value = query_heads.shape[2] ** (-0.5)
    allowed = (query_seq == key_seq) & (key_pos[None, :] <= query_pos[:, None])
    distance = jnp.maximum(query_pos[:, None] - key_pos[None, :], 0).astype(jnp.float32)
    denom = jnp.log1p(jnp.maximum(query_pos.astype(jnp.float32), fire_floor))
    ratio = jnp.log1p(distance) / denom[:, None]
    hidden_pre = fire_w1[:, None, None] * ratio[None] + fire_b1[:, None, None]
    hidden_act = jnp.maximum(hidden_pre, 0.0)
    pair_bias = jnp.einsum("cqk,ch->hqk", hidden_act, fire_w2, precision=highest)
    scores = (
        jnp.einsum("qhd,khd->hqk", query_heads, key_heads, preferred_element_type=jnp.float32)
        * scale_value
        + pair_bias
    )
    shifted = jnp.where(allowed[None], scores - log_block.T[:, :, None], -1e30)
    prob_block = jnp.exp(shifted)
    dprob = jnp.einsum("qhd,khd->hqk", grad_heads, value_heads, preferred_element_type=jnp.float32)
    dscore = prob_block * (dprob - delta_block.T[:, :, None])
    prob_low = prob_block.astype(jnp.bfloat16)
    score_low = dscore.astype(jnp.bfloat16)
    grad_query = (
        jnp.einsum("hqk,khd->qhd", score_low, key_heads, preferred_element_type=jnp.float32)
        * scale_value
    )
    grad_key = (
        jnp.einsum("hqk,qhd->khd", score_low, query_heads, preferred_element_type=jnp.float32)
        * scale_value
    )
    grad_value = jnp.einsum(
        "hqk,qhd->khd", prob_low, grad_heads, preferred_element_type=jnp.float32
    )
    grad_second = jnp.einsum("hqk,cqk->ch", dscore, hidden_act, precision=highest)
    grad_act = jnp.einsum("hqk,ch->cqk", dscore, fire_w2, precision=highest)
    grad_pre = jnp.where(hidden_pre > 0, grad_act, 0.0)
    grad_first = jnp.sum(grad_pre * ratio[None], axis=(1, 2))
    grad_bias = jnp.sum(grad_pre, axis=(1, 2))
    return (grad_query, grad_key, grad_value, grad_first, grad_bias, grad_second)


def sent_back(block, axis, distance):
    count = lax.axis_size(axis)
    return lax.ppermute(block, axis, [(i, i - distance) for i in range(distance, count)])


def sent_forward(block, axis, distance):
    count = lax.axis_size(axis)
    return lax.ppermute(block, axis, [(i, i + distance) for i in range(count - distance)])


def on_device(queries, keys, values, outputs, d_out, log_norm, lengths, fire_w1, fire_b1, fire_w2):
    rows_dev = queries.shape[1]
    heads_count = log_norm.shape[2]
    feature_count = queries.shape[2]
    head_size = feature_count // heads_count
    cp_count = lax.axis_size("cp")
    my_index = lax.axis_index("cp")
    length_row = lengths[0]
    query_heads = queries[0].reshape(rows_dev, heads_count, head_size)
    key_heads = keys[0].reshape(rows_dev, heads_count, head_size)
    value_heads = values[0].reshape(rows_dev, heads_count, head_size)
    grad_heads = d_out[0].reshape(rows_dev, heads_count, head_size)
    out_heads = outputs[0].reshape(rows_dev, heads_count, head_size)
    log_block = log_norm[0]
    delta_block = jnp.einsum(
        "qhd,qhd->qh", grad_heads, out_heads, preferred_element_type=jnp.float32
    )
    token_index = jnp.arange(rows_dev, dtype=jnp.int32)

    def seat_positions(device):
        sequence, offset = seat_of(length_row, device)
        return (sequence, offset * rows_dev + token_index)

    my_seq, my_pos = seat_positions(my_index)
    query_side = jnp.stack([query_heads, grad_heads])
    stats_side = jnp.stack([log_block, delta_block])
    arrived = [
        (sent_back(query_side, "cp", hop), sent_back(stats_side, "cp", hop))
        for hop in range(1, GROUP_MOST)
    ]
    local = pair_terms(
        query_heads,
        grad_heads,
        log_block,
        delta_block,
        key_heads,
        value_heads,
        my_seq,
        my_pos,
        my_seq,
        my_pos,
        fire_w1,
        fire_b1,
        fire_w2,
    )
    grad_q, grad_k, grad_v, first, bias_sum, second = local
    returned = []
    for hop in range(1, GROUP_MOST):
        far_query, far_stats = arrived[hop - 1]
        query_seq, query_pos = seat_positions(my_index + hop)
        terms = pair_terms(
            far_query[0],
            far_query[1],
            far_stats[0],
            far_stats[1],
            key_heads,
            value_heads,
            query_seq,
            query_pos,
            my_seq,
            my_pos,
            fire_w1,
            fire_b1,
            fire_w2,
        )
        grad_k = grad_k + terms[1]
        grad_v = grad_v + terms[2]
        first = first + terms[3]
        bias_sum = bias_sum + terms[4]
        second = second + terms[5]
        returned.append(sent_forward(terms[0], "cp", hop))
    for part in returned:
        grad_q = grad_q + part
    hid = first.shape[0]
    flat = jnp.concatenate([first, bias_sum, second.reshape(-1)])
    flat = lax.psum(flat, ("cp", "dp"))
    first, bias_sum, second = flat[:hid], flat[hid : 2 * hid], flat[2 * hid :].reshape(second.shape)
    factor = (lax.axis_size("dp") * cp_count * rows_dev) ** (-0.5)
    out_shape = (1, rows_dev, feature_count)
    return (
        grad_q.reshape(out_shape).astype(jnp.bfloat16),
        grad_k.reshape(out_shape).astype(jnp.bfloat16),
        grad_v.reshape(out_shape).astype(jnp.bfloat16),
        first * factor,
        bias_sum * factor,
        second * factor,
    )


def solution(mesh):
    placed = (
        P("dp", "cp", None),
        P("dp", "cp", None),
        P("dp", "cp", None),
        P("dp", "cp", None),
        P("dp", "cp", None),
        P("dp", "cp", None),
        P("dp", None),
        P(),
        P(),
        P(),
    )
    return jax.shard_map(
        on_device,
        mesh=mesh,
        in_specs=placed,
        out_specs=(P("dp", "cp", None), P("dp", "cp", None), P("dp", "cp", None), P(), P(), P()),
        check_vma=False,
    )
```

```python
import jax
import jax.numpy as jnp
from jax import lax
from jax.sharding import PartitionSpec as P

GROUP_MOST = 4


fire_floor = 64.0


def shifted_2(block, axis, distance):
    devices = range(lax.axis_size(axis))
    route = [(i - distance, i) for i in devices if i - distance in devices]
    return lax.ppermute(block, axis, route)


def shifted_3(shard, axis, by):
    count = lax.axis_size(axis)
    return lax.ppermute(shard, axis, [(i, (i + by) % count) for i in range(count)])


def seat_of(length_row, device):
    ends = jnp.cumsum(length_row)
    sequence = jnp.sum((ends <= device).astype(jnp.int32))
    before = jnp.sum(
        jnp.where(jnp.arange(length_row.shape[0], dtype=jnp.int32) < sequence, length_row, 0)
    )
    return (sequence, device - before)


def pair_terms(
    query_heads,
    grad_heads,
    log_block,
    delta_block,
    key_heads,
    value_heads,
    query_seq,
    query_pos,
    key_seq,
    key_pos,
    fire_w1,
    fire_b1,
    fire_w2,
):
    highest = lax.Precision.HIGHEST
    scale_value = query_heads.shape[2] ** (-0.5)
    allowed = (query_seq == key_seq) & (key_pos[None, :] <= query_pos[:, None])
    distance = jnp.maximum(query_pos[:, None] - key_pos[None, :], 0).astype(jnp.float32)
    denom = jnp.log1p(jnp.maximum(query_pos.astype(jnp.float32), fire_floor))
    ratio = jnp.log1p(distance) / denom[:, None]
    hidden_pre = fire_w1[:, None, None] * ratio[None] + fire_b1[:, None, None]
    hidden_act = jnp.maximum(hidden_pre, 0.0)
    pair_bias = jnp.einsum("cqk,ch->hqk", hidden_act, fire_w2, precision=highest)
    scores = (
        jnp.einsum("qhd,khd->hqk", query_heads, key_heads, preferred_element_type=jnp.float32)
        * scale_value
        + pair_bias
    )
    shifted = jnp.where(allowed[None], scores - log_block.T[:, :, None], -1e30)
    prob_block = jnp.exp(shifted)
    dprob = jnp.einsum("qhd,khd->hqk", grad_heads, value_heads, preferred_element_type=jnp.float32)
    dscore = prob_block * (dprob - delta_block.T[:, :, None])
    prob_low = prob_block.astype(jnp.bfloat16)
    score_low = dscore.astype(jnp.bfloat16)
    grad_query = (
        jnp.einsum("hqk,khd->qhd", score_low, key_heads, preferred_element_type=jnp.float32)
        * scale_value
    )
    grad_key = (
        jnp.einsum("hqk,qhd->khd", score_low, query_heads, preferred_element_type=jnp.float32)
        * scale_value
    )
    grad_value = jnp.einsum(
        "hqk,qhd->khd", prob_low, grad_heads, preferred_element_type=jnp.float32
    )
    grad_second = jnp.einsum("hqk,cqk->ch", dscore, hidden_act, precision=highest)
    grad_act = jnp.einsum("hqk,ch->cqk", dscore, fire_w2, precision=highest)
    grad_pre = jnp.where(hidden_pre > 0, grad_act, 0.0)
    grad_first = jnp.sum(grad_pre * ratio[None], axis=(1, 2))
    grad_bias = jnp.sum(grad_pre, axis=(1, 2))
    return (grad_query, grad_key, grad_value, grad_first, grad_bias, grad_second)


def sent_back(block, axis, distance):
    count = lax.axis_size(axis)
    return lax.ppermute(block, axis, [(i, i - distance) for i in range(distance, count)])


def sent_forward(block, axis, distance):
    count = lax.axis_size(axis)
    return lax.ppermute(block, axis, [(i, i + distance) for i in range(count - distance)])


def butterfly_sum(block, axes):
    for axis in axes:
        count = lax.axis_size(axis)
        step = 1
        while step < count:
            block = block + lax.ppermute(block, axis, [(i, i ^ step) for i in range(count)])
            step *= 2
    return block


def on_device(queries, keys, values, outputs, d_out, log_norm, lengths, fire_w1, fire_b1, fire_w2):
    rows_dev = queries.shape[1]
    heads_count = log_norm.shape[2]
    feature_count = queries.shape[2]
    head_size = feature_count // heads_count
    cp_count = lax.axis_size("cp")
    my_index = lax.axis_index("cp")
    length_row = lengths[0]
    query_heads = queries[0].reshape(rows_dev, heads_count, head_size)
    key_heads = keys[0].reshape(rows_dev, heads_count, head_size)
    value_heads = values[0].reshape(rows_dev, heads_count, head_size)
    grad_heads = d_out[0].reshape(rows_dev, heads_count, head_size)
    out_heads = outputs[0].reshape(rows_dev, heads_count, head_size)
    log_block = log_norm[0]
    delta_block = jnp.einsum(
        "qhd,qhd->qh", grad_heads, out_heads, preferred_element_type=jnp.float32
    )
    token_index = jnp.arange(rows_dev, dtype=jnp.int32)

    def seat_positions(device):
        sequence, offset = seat_of(length_row, device)
        return (sequence, offset * rows_dev + token_index)

    my_seq, my_pos = seat_positions(my_index)
    query_side = jnp.stack([query_heads, grad_heads])
    stats_side = jnp.stack([log_block, delta_block])
    arrived = [
        (sent_back(query_side, "cp", hop), sent_back(stats_side, "cp", hop))
        for hop in range(1, GROUP_MOST)
    ]
    local = pair_terms(
        query_heads,
        grad_heads,
        log_block,
        delta_block,
        key_heads,
        value_heads,
        my_seq,
        my_pos,
        my_seq,
        my_pos,
        fire_w1,
        fire_b1,
        fire_w2,
    )
    grad_q, grad_k, grad_v, first, bias_sum, second = local
    returned = []
    for hop in range(1, GROUP_MOST):
        far_query, far_stats = arrived[hop - 1]
        query_seq, query_pos = seat_positions(my_index + hop)
        terms = pair_terms(
            far_query[0],
            far_query[1],
            far_stats[0],
            far_stats[1],
            key_heads,
            value_heads,
            query_seq,
            query_pos,
            my_seq,
            my_pos,
            fire_w1,
            fire_b1,
            fire_w2,
        )
        grad_k = grad_k + terms[1]
        grad_v = grad_v + terms[2]
        first = first + terms[3]
        bias_sum = bias_sum + terms[4]
        second = second + terms[5]
        returned.append(sent_forward(terms[0].astype(jnp.bfloat16), "cp", hop))
    for part in returned:
        grad_q = grad_q + part.astype(jnp.float32)
    hid = first.shape[0]
    flat = jnp.concatenate([first, bias_sum, second.reshape(-1)])
    flat = butterfly_sum(flat, ("cp", "dp"))
    first, bias_sum, second = flat[:hid], flat[hid : 2 * hid], flat[2 * hid :].reshape(second.shape)
    factor = (lax.axis_size("dp") * cp_count * rows_dev) ** (-0.5)
    out_shape = (1, rows_dev, feature_count)
    return (
        grad_q.reshape(out_shape).astype(jnp.bfloat16),
        grad_k.reshape(out_shape).astype(jnp.bfloat16),
        grad_v.reshape(out_shape).astype(jnp.bfloat16),
        first * factor,
        bias_sum * factor,
        second * factor,
    )


def solution(mesh):
    placed = (
        P("dp", "cp", None),
        P("dp", "cp", None),
        P("dp", "cp", None),
        P("dp", "cp", None),
        P("dp", "cp", None),
        P("dp", "cp", None),
        P("dp", None),
        P(),
        P(),
        P(),
    )
    return jax.shard_map(
        on_device,
        mesh=mesh,
        in_specs=placed,
        out_specs=(P("dp", "cp", None), P("dp", "cp", None), P("dp", "cp", None), P(), P(), P()),
        check_vma=False,
    )
```

```python
import jax
import jax.numpy as jnp
from jax import lax
from jax.sharding import PartitionSpec as P

GROUP_MOST = 4


fire_floor = 64.0


def shifted_2(block, axis, distance):
    devices = range(lax.axis_size(axis))
    route = [(i - distance, i) for i in devices if i - distance in devices]
    return lax.ppermute(block, axis, route)


def shifted_3(shard, axis, by):
    count = lax.axis_size(axis)
    return lax.ppermute(shard, axis, [(i, (i + by) % count) for i in range(count)])


def seat_of(length_row, device):
    ends = jnp.cumsum(length_row)
    sequence = jnp.sum((ends <= device).astype(jnp.int32))
    before = jnp.sum(
        jnp.where(jnp.arange(length_row.shape[0], dtype=jnp.int32) < sequence, length_row, 0)
    )
    return (sequence, device - before)


def position_terms(query_seq, query_pos, key_seq, key_pos, fire_w1, fire_b1, fire_w2):
    highest = lax.Precision.HIGHEST
    allowed = (query_seq == key_seq) & (key_pos[None, :] <= query_pos[:, None])
    distance = jnp.maximum(query_pos[:, None] - key_pos[None, :], 0).astype(jnp.float32)
    denom = jnp.log1p(jnp.maximum(query_pos.astype(jnp.float32), fire_floor))
    ratio = jnp.log1p(distance) / denom[:, None]
    hidden_pre = fire_w1[:, None, None] * ratio[None] + fire_b1[:, None, None]
    hidden_act = jnp.maximum(hidden_pre, 0.0)
    pair_bias = jnp.einsum("cqk,ch->hqk", hidden_act, fire_w2, precision=highest)
    return (allowed, ratio, hidden_pre, hidden_act, pair_bias)


def pair_terms(
    query_heads,
    grad_heads,
    log_block,
    delta_block,
    key_heads,
    value_heads,
    positional,
    fire_w2,
):
    highest = lax.Precision.HIGHEST
    allowed, ratio, hidden_pre, hidden_act, pair_bias = positional
    scale_value = query_heads.shape[2] ** (-0.5)
    scores = (
        jnp.einsum("qhd,khd->hqk", query_heads, key_heads, preferred_element_type=jnp.float32)
        * scale_value
        + pair_bias
    )
    shifted = jnp.where(allowed[None], scores - log_block.T[:, :, None], -1e30)
    prob_block = jnp.exp(shifted)
    dprob = jnp.einsum("qhd,khd->hqk", grad_heads, value_heads, preferred_element_type=jnp.float32)
    dscore = prob_block * (dprob - delta_block.T[:, :, None])
    prob_low = prob_block.astype(jnp.bfloat16)
    score_low = dscore.astype(jnp.bfloat16)
    grad_query = (
        jnp.einsum("hqk,khd->qhd", score_low, key_heads, preferred_element_type=jnp.float32)
        * scale_value
    )
    grad_key = (
        jnp.einsum("hqk,qhd->khd", score_low, query_heads, preferred_element_type=jnp.float32)
        * scale_value
    )
    grad_value = jnp.einsum(
        "hqk,qhd->khd", prob_low, grad_heads, preferred_element_type=jnp.float32
    )
    grad_second = jnp.einsum("hqk,cqk->ch", dscore, hidden_act, precision=highest)
    grad_act = jnp.einsum("hqk,ch->cqk", dscore, fire_w2, precision=highest)
    grad_pre = jnp.where(hidden_pre > 0, grad_act, 0.0)
    grad_first = jnp.sum(grad_pre * ratio[None], axis=(1, 2))
    grad_bias = jnp.sum(grad_pre, axis=(1, 2))
    return (grad_query, grad_key, grad_value, grad_first, grad_bias, grad_second)


def sent_back(block, axis, distance):
    count = lax.axis_size(axis)
    return lax.ppermute(block, axis, [(i, i - distance) for i in range(distance, count)])


def sent_forward(block, axis, distance):
    count = lax.axis_size(axis)
    return lax.ppermute(block, axis, [(i, i + distance) for i in range(count - distance)])


def radix_sum(block, axes):
    for axis in axes:
        count = lax.axis_size(axis)
        me = lax.axis_index(axis)
        stride = 1
        while stride < count:
            width = min(4, count // stride)
            digit = (me // stride) % width

            def moved(i, shift):
                d = (i // stride) % width
                return i + ((d + shift) % width - d) * stride

            got = [block] + [
                lax.ppermute(block, axis, [(i, moved(i, shift)) for i in range(count)])
                for shift in range(1, width)
            ]
            stacked = jnp.stack(got)
            ordered = [stacked[(digit - t) % width] for t in range(width)]
            total = ordered[0]
            for part in ordered[1:]:
                total = total + part
            block = total
            stride *= width
    return block


def on_device(queries, keys, values, outputs, d_out, log_norm, lengths, fire_w1, fire_b1, fire_w2):
    rows_dev = queries.shape[1]
    heads_count = log_norm.shape[2]
    feature_count = queries.shape[2]
    head_size = feature_count // heads_count
    cp_count = lax.axis_size("cp")
    my_index = lax.axis_index("cp")
    length_row = lengths[0]
    query_heads = queries[0].reshape(rows_dev, heads_count, head_size)
    key_heads = keys[0].reshape(rows_dev, heads_count, head_size)
    value_heads = values[0].reshape(rows_dev, heads_count, head_size)
    grad_heads = d_out[0].reshape(rows_dev, heads_count, head_size)
    out_heads = outputs[0].reshape(rows_dev, heads_count, head_size)
    log_block = log_norm[0]
    delta_block = jnp.einsum(
        "qhd,qhd->qh", grad_heads, out_heads, preferred_element_type=jnp.float32
    )
    token_index = jnp.arange(rows_dev, dtype=jnp.int32)

    def seat_positions(device):
        sequence, offset = seat_of(length_row, device)
        return (sequence, offset * rows_dev + token_index)

    my_seq, my_pos = seat_positions(my_index)
    query_side = jnp.stack([query_heads, grad_heads])
    stats_side = jnp.stack([log_block, delta_block])
    arrived = {
        hop: (sent_back(query_side, "cp", hop), sent_back(stats_side, "cp", hop))
        for hop in range(1, GROUP_MOST)
    }
    positional = {}
    for hop in range(GROUP_MOST):
        query_seq, query_pos = seat_positions(my_index + hop)
        positional[hop] = position_terms(
            query_seq, query_pos, my_seq, my_pos, fire_w1, fire_b1, fire_w2
        )
    local = pair_terms(
        query_heads,
        grad_heads,
        log_block,
        delta_block,
        key_heads,
        value_heads,
        positional[0],
        fire_w2,
    )
    grad_q, grad_k, grad_v, first, bias_sum, second = local
    returned = []
    order = [2, 1] + list(range(3, GROUP_MOST))
    for hop in order:
        (far_query, far_stats), positional[hop], grad_k, grad_v = lax.optimization_barrier(
            (arrived[hop], positional[hop], grad_k, grad_v)
        )
        terms = pair_terms(
            far_query[0],
            far_query[1],
            far_stats[0],
            far_stats[1],
            key_heads,
            value_heads,
            positional[hop],
            fire_w2,
        )
        grad_k = grad_k + terms[1]
        grad_v = grad_v + terms[2]
        first = first + terms[3]
        bias_sum = bias_sum + terms[4]
        second = second + terms[5]
        returned.append(sent_forward(terms[0].astype(jnp.bfloat16), "cp", hop))
    for part in returned:
        grad_q = grad_q + part.astype(jnp.float32)
    hid = first.shape[0]
    flat = jnp.concatenate([first, bias_sum, second.reshape(-1)])
    flat = radix_sum(flat, ("cp", "dp"))
    first, bias_sum, second = flat[:hid], flat[hid : 2 * hid], flat[2 * hid :].reshape(second.shape)
    factor = (lax.axis_size("dp") * cp_count * rows_dev) ** (-0.5)
    out_shape = (1, rows_dev, feature_count)
    return (
        grad_q.reshape(out_shape).astype(jnp.bfloat16),
        grad_k.reshape(out_shape).astype(jnp.bfloat16),
        grad_v.reshape(out_shape).astype(jnp.bfloat16),
        first * factor,
        bias_sum * factor,
        second * factor,
    )


def solution(mesh):
    placed = (
        P("dp", "cp", None),
        P("dp", "cp", None),
        P("dp", "cp", None),
        P("dp", "cp", None),
        P("dp", "cp", None),
        P("dp", "cp", None),
        P("dp", None),
        P(),
        P(),
        P(),
    )
    return jax.shard_map(
        on_device,
        mesh=mesh,
        in_specs=placed,
        out_specs=(P("dp", "cp", None), P("dp", "cp", None), P("dp", "cp", None), P(), P(), P()),
        check_vma=False,
    )
```

```python
import jax
import jax.numpy as jnp
from jax import lax
from jax.sharding import PartitionSpec as P

GROUP_MOST = 4

KEY_HOPS = (2,)


fire_floor = 64.0


def shifted_2(block, axis, distance):
    devices = range(lax.axis_size(axis))
    route = [(i - distance, i) for i in devices if i - distance in devices]
    return lax.ppermute(block, axis, route)


def shifted_3(shard, axis, by):
    count = lax.axis_size(axis)
    return lax.ppermute(shard, axis, [(i, (i + by) % count) for i in range(count)])


def seat_of(length_row, device):
    ends = jnp.cumsum(length_row)
    sequence = jnp.sum((ends <= device).astype(jnp.int32))
    before = jnp.sum(
        jnp.where(jnp.arange(length_row.shape[0], dtype=jnp.int32) < sequence, length_row, 0)
    )
    return (sequence, device - before)


def position_terms(query_seq, query_pos, key_seq, key_pos, fire_w1, fire_b1, fire_w2):
    highest = lax.Precision.HIGHEST
    allowed = (query_seq == key_seq) & (key_pos[None, :] <= query_pos[:, None])
    distance = jnp.maximum(query_pos[:, None] - key_pos[None, :], 0).astype(jnp.float32)
    denom = jnp.log1p(jnp.maximum(query_pos.astype(jnp.float32), fire_floor))
    ratio = jnp.log1p(distance) / denom[:, None]
    hidden_pre = fire_w1[:, None, None] * ratio[None] + fire_b1[:, None, None]
    hidden_act = jnp.maximum(hidden_pre, 0.0)
    pair_bias = jnp.einsum("cqk,ch->hqk", hidden_act, fire_w2, precision=highest)
    return (allowed, ratio, hidden_pre, hidden_act, pair_bias)


def pair_terms(
    query_heads,
    grad_heads,
    log_block,
    delta_block,
    key_heads,
    value_heads,
    positional,
    fire_w2,
):
    highest = lax.Precision.HIGHEST
    allowed, ratio, hidden_pre, hidden_act, pair_bias = positional
    scale_value = query_heads.shape[2] ** (-0.5)
    scores = (
        jnp.einsum("qhd,khd->hqk", query_heads, key_heads, preferred_element_type=jnp.float32)
        * scale_value
        + pair_bias
    )
    shifted = jnp.where(allowed[None], scores - log_block.T[:, :, None], -1e30)
    prob_block = jnp.exp(shifted)
    dprob = jnp.einsum("qhd,khd->hqk", grad_heads, value_heads, preferred_element_type=jnp.float32)
    dscore = prob_block * (dprob - delta_block.T[:, :, None])
    prob_low = prob_block.astype(jnp.bfloat16)
    score_low = dscore.astype(jnp.bfloat16)
    grad_query = (
        jnp.einsum("hqk,khd->qhd", score_low, key_heads, preferred_element_type=jnp.float32)
        * scale_value
    )
    grad_key = (
        jnp.einsum("hqk,qhd->khd", score_low, query_heads, preferred_element_type=jnp.float32)
        * scale_value
    )
    grad_value = jnp.einsum(
        "hqk,qhd->khd", prob_low, grad_heads, preferred_element_type=jnp.float32
    )
    grad_second = jnp.einsum("hqk,cqk->ch", dscore, hidden_act, precision=highest)
    grad_act = jnp.einsum("hqk,ch->cqk", dscore, fire_w2, precision=highest)
    grad_pre = jnp.where(hidden_pre > 0, grad_act, 0.0)
    grad_first = jnp.sum(grad_pre * ratio[None], axis=(1, 2))
    grad_bias = jnp.sum(grad_pre, axis=(1, 2))
    return (grad_query, grad_key, grad_value, grad_first, grad_bias, grad_second)


def sent_back(block, axis, distance):
    count = lax.axis_size(axis)
    return lax.ppermute(block, axis, [(i, i - distance) for i in range(distance, count)])


def sent_forward(block, axis, distance):
    count = lax.axis_size(axis)
    return lax.ppermute(block, axis, [(i, i + distance) for i in range(count - distance)])


def radix_sum(block, axes):
    for axis in axes:
        count = lax.axis_size(axis)
        me = lax.axis_index(axis)
        stride = 1
        while stride < count:
            width = min(4, count // stride)
            digit = (me // stride) % width

            def moved(i, shift):
                d = (i // stride) % width
                return i + ((d + shift) % width - d) * stride

            got = [block] + [
                lax.ppermute(block, axis, [(i, moved(i, shift)) for i in range(count)])
                for shift in range(1, width)
            ]
            stacked = jnp.stack(got)
            ordered = [stacked[(digit - t) % width] for t in range(width)]
            total = ordered[0]
            for part in ordered[1:]:
                total = total + part
            block = total
            stride *= width
    return block


def on_device(queries, keys, values, outputs, d_out, log_norm, lengths, fire_w1, fire_b1, fire_w2):
    rows_dev = queries.shape[1]
    heads_count = log_norm.shape[2]
    feature_count = queries.shape[2]
    head_size = feature_count // heads_count
    cp_count = lax.axis_size("cp")
    my_index = lax.axis_index("cp")
    length_row = lengths[0]
    query_heads = queries[0].reshape(rows_dev, heads_count, head_size)
    key_heads = keys[0].reshape(rows_dev, heads_count, head_size)
    value_heads = values[0].reshape(rows_dev, heads_count, head_size)
    grad_heads = d_out[0].reshape(rows_dev, heads_count, head_size)
    out_heads = outputs[0].reshape(rows_dev, heads_count, head_size)
    log_block = log_norm[0]
    delta_block = jnp.einsum(
        "qhd,qhd->qh", grad_heads, out_heads, preferred_element_type=jnp.float32
    )
    token_index = jnp.arange(rows_dev, dtype=jnp.int32)

    def seat_positions(device):
        sequence, offset = seat_of(length_row, device)
        return (sequence, offset * rows_dev + token_index)

    my_seq, my_pos = seat_positions(my_index)
    query_side = jnp.stack([query_heads, grad_heads])
    stats_side = jnp.stack([log_block, delta_block])
    key_side = jnp.stack([key_heads, value_heads])
    arrived = {}
    positional = {}
    for hop in range(1, GROUP_MOST):
        if hop in KEY_HOPS:
            arrived[hop] = sent_forward(key_side, "cp", hop)
            key_seq, key_pos = seat_positions((my_index - hop) % cp_count)
            key_seq = jnp.where(my_index >= hop, key_seq, -1)
            positional[hop] = position_terms(
                my_seq, my_pos, key_seq, key_pos, fire_w1, fire_b1, fire_w2
            )
        else:
            arrived[hop] = (sent_back(query_side, "cp", hop), sent_back(stats_side, "cp", hop))
            query_seq, query_pos = seat_positions(my_index + hop)
            query_seq = jnp.where(my_index + hop < cp_count, query_seq, -2)
            positional[hop] = position_terms(
                query_seq, query_pos, my_seq, my_pos, fire_w1, fire_b1, fire_w2
            )
    positional[0] = position_terms(my_seq, my_pos, my_seq, my_pos, fire_w1, fire_b1, fire_w2)
    local = pair_terms(
        query_heads,
        grad_heads,
        log_block,
        delta_block,
        key_heads,
        value_heads,
        positional[0],
        fire_w2,
    )
    grad_q, grad_k, grad_v, first, bias_sum, second = local
    returned_q = []
    returned_kv = []
    order = [2, 1] + list(range(3, GROUP_MOST))
    for hop in order:
        got, positional[hop], grad_q, grad_k, grad_v = lax.optimization_barrier(
            (arrived[hop], positional[hop], grad_q, grad_k, grad_v)
        )
        if hop in KEY_HOPS:
            terms = pair_terms(
                query_heads,
                grad_heads,
                log_block,
                delta_block,
                got[0],
                got[1],
                positional[hop],
                fire_w2,
            )
            grad_q = grad_q + terms[0]
            partial = jnp.stack([terms[1], terms[2]]).astype(jnp.bfloat16)
            returned_kv.append(sent_back(partial, "cp", hop))
        else:
            far_query, far_stats = got
            terms = pair_terms(
                far_query[0],
                far_query[1],
                far_stats[0],
                far_stats[1],
                key_heads,
                value_heads,
                positional[hop],
                fire_w2,
            )
            grad_k = grad_k + terms[1]
            grad_v = grad_v + terms[2]
            returned_q.append(sent_forward(terms[0].astype(jnp.bfloat16), "cp", hop))
        first = first + terms[3]
        bias_sum = bias_sum + terms[4]
        second = second + terms[5]
    for part in returned_q:
        grad_q = grad_q + part.astype(jnp.float32)
    for part in returned_kv:
        grad_k = grad_k + part[0].astype(jnp.float32)
        grad_v = grad_v + part[1].astype(jnp.float32)
    hid = first.shape[0]
    flat = jnp.concatenate([first, bias_sum, second.reshape(-1)])
    flat = radix_sum(flat, ("cp", "dp"))
    first, bias_sum, second = flat[:hid], flat[hid : 2 * hid], flat[2 * hid :].reshape(second.shape)
    factor = (lax.axis_size("dp") * cp_count * rows_dev) ** (-0.5)
    out_shape = (1, rows_dev, feature_count)
    return (
        grad_q.reshape(out_shape).astype(jnp.bfloat16),
        grad_k.reshape(out_shape).astype(jnp.bfloat16),
        grad_v.reshape(out_shape).astype(jnp.bfloat16),
        first * factor,
        bias_sum * factor,
        second * factor,
    )


def solution(mesh):
    placed = (
        P("dp", "cp", None),
        P("dp", "cp", None),
        P("dp", "cp", None),
        P("dp", "cp", None),
        P("dp", "cp", None),
        P("dp", "cp", None),
        P("dp", None),
        P(),
        P(),
        P(),
    )
    return jax.shard_map(
        on_device,
        mesh=mesh,
        in_specs=placed,
        out_specs=(P("dp", "cp", None), P("dp", "cp", None), P("dp", "cp", None), P(), P(), P()),
        check_vma=False,
    )
```

```python
import jax
import jax.numpy as jnp
from jax import lax
from jax.sharding import PartitionSpec as P

GROUP_MOST = 4

KEY_HOPS = (2,)


fire_floor = 64.0


def shifted_2(block, axis, distance):
    devices = range(lax.axis_size(axis))
    route = [(i - distance, i) for i in devices if i - distance in devices]
    return lax.ppermute(block, axis, route)


def shifted_3(shard, axis, by):
    count = lax.axis_size(axis)
    return lax.ppermute(shard, axis, [(i, (i + by) % count) for i in range(count)])


def seat_of(length_row, device):
    ends = jnp.cumsum(length_row)
    sequence = jnp.sum((ends <= device).astype(jnp.int32))
    before = jnp.sum(
        jnp.where(jnp.arange(length_row.shape[0], dtype=jnp.int32) < sequence, length_row, 0)
    )
    return (sequence, device - before)


def position_terms(query_seq, query_pos, key_seq, key_pos, fire_w1, fire_b1, fire_w2):
    allowed = (query_seq == key_seq) & (key_pos[None, :] <= query_pos[:, None])
    distance = jnp.maximum(query_pos[:, None] - key_pos[None, :], 0).astype(jnp.float32)
    denom = jnp.log1p(jnp.maximum(query_pos.astype(jnp.float32), fire_floor))
    ratio = jnp.log1p(distance) / denom[:, None]
    hidden_pre = fire_w1[:, None, None] * ratio[None] + fire_b1[:, None, None]
    hidden_act = jnp.maximum(hidden_pre, 0.0)
    pair_bias = jnp.einsum("cqk,ch->hqk", hidden_act, fire_w2, precision=lax.Precision.HIGH)
    live = (hidden_pre > 0).astype(jnp.float32)
    fire_basis = jnp.concatenate([live, live * ratio[None]], axis=0)
    return (allowed, pair_bias, fire_basis)


def pair_terms(
    query_heads,
    grad_heads,
    log_block,
    delta_block,
    key_heads,
    value_heads,
    positional,
    fire_w2,
):
    allowed, pair_bias, fire_basis = positional
    scale_value = query_heads.shape[2] ** (-0.5)
    scores = (
        jnp.einsum("qhd,khd->hqk", query_heads, key_heads, preferred_element_type=jnp.float32)
        * scale_value
        + pair_bias
    )
    shifted = jnp.where(allowed[None], scores - log_block.T[:, :, None], -1e30)
    prob_block = jnp.exp(shifted)
    dprob = jnp.einsum("qhd,khd->hqk", grad_heads, value_heads, preferred_element_type=jnp.float32)
    dscore = prob_block * (dprob - delta_block.T[:, :, None])
    prob_low = prob_block.astype(jnp.bfloat16)
    score_low = dscore.astype(jnp.bfloat16)
    grad_query = (
        jnp.einsum("hqk,khd->qhd", score_low, key_heads, preferred_element_type=jnp.float32)
        * scale_value
    )
    grad_key = (
        jnp.einsum("hqk,qhd->khd", score_low, query_heads, preferred_element_type=jnp.float32)
        * scale_value
    )
    grad_value = jnp.einsum(
        "hqk,qhd->khd", prob_low, grad_heads, preferred_element_type=jnp.float32
    )
    moments = jnp.einsum("hqk,mqk->mh", dscore, fire_basis, precision=lax.Precision.HIGH)
    return (grad_query, grad_key, grad_value, moments)


def sent_back(block, axis, distance):
    count = lax.axis_size(axis)
    return lax.ppermute(block, axis, [(i, i - distance) for i in range(distance, count)])


def sent_forward(block, axis, distance):
    count = lax.axis_size(axis)
    return lax.ppermute(block, axis, [(i, i + distance) for i in range(count - distance)])


def radix_sum(block, axes):
    for axis in axes:
        count = lax.axis_size(axis)
        me = lax.axis_index(axis)
        stride = 1
        while stride < count:
            width = min(4, count // stride)
            digit = (me // stride) % width

            def moved(i, shift):
                d = (i // stride) % width
                return i + ((d + shift) % width - d) * stride

            got = [block] + [
                lax.ppermute(block, axis, [(i, moved(i, shift)) for i in range(count)])
                for shift in range(1, width)
            ]
            stacked = jnp.stack(got)
            ordered = [stacked[(digit - t) % width] for t in range(width)]
            total = ordered[0]
            for part in ordered[1:]:
                total = total + part
            block = total
            stride *= width
    return block


def on_device(queries, keys, values, outputs, d_out, log_norm, lengths, fire_w1, fire_b1, fire_w2):
    rows_dev = queries.shape[1]
    heads_count = log_norm.shape[2]
    feature_count = queries.shape[2]
    head_size = feature_count // heads_count
    cp_count = lax.axis_size("cp")
    my_index = lax.axis_index("cp")
    length_row = lengths[0]
    query_heads = queries[0].reshape(rows_dev, heads_count, head_size)
    key_heads = keys[0].reshape(rows_dev, heads_count, head_size)
    value_heads = values[0].reshape(rows_dev, heads_count, head_size)
    grad_heads = d_out[0].reshape(rows_dev, heads_count, head_size)
    out_heads = outputs[0].reshape(rows_dev, heads_count, head_size)
    log_block = log_norm[0]
    delta_block = jnp.einsum(
        "qhd,qhd->qh", grad_heads, out_heads, preferred_element_type=jnp.float32
    )
    token_index = jnp.arange(rows_dev, dtype=jnp.int32)

    def seat_positions(device):
        sequence, offset = seat_of(length_row, device)
        return (sequence, offset * rows_dev + token_index)

    my_seq, my_pos = seat_positions(my_index)
    query_side = jnp.stack([query_heads, grad_heads])
    stats_side = jnp.stack([log_block, delta_block])
    key_side = jnp.stack([key_heads, value_heads])
    arrived = {}
    positional = {}
    for hop in range(1, GROUP_MOST):
        if hop in KEY_HOPS:
            arrived[hop] = sent_forward(key_side, "cp", hop)
            key_seq, key_pos = seat_positions((my_index - hop) % cp_count)
            key_seq = jnp.where(my_index >= hop, key_seq, -1)
            positional[hop] = position_terms(
                my_seq, my_pos, key_seq, key_pos, fire_w1, fire_b1, fire_w2
            )
        else:
            arrived[hop] = (sent_back(query_side, "cp", hop), sent_back(stats_side, "cp", hop))
            query_seq, query_pos = seat_positions(my_index + hop)
            query_seq = jnp.where(my_index + hop < cp_count, query_seq, -2)
            positional[hop] = position_terms(
                query_seq, query_pos, my_seq, my_pos, fire_w1, fire_b1, fire_w2
            )
    positional[0] = position_terms(my_seq, my_pos, my_seq, my_pos, fire_w1, fire_b1, fire_w2)
    local = pair_terms(
        query_heads,
        grad_heads,
        log_block,
        delta_block,
        key_heads,
        value_heads,
        positional[0],
        fire_w2,
    )
    grad_q, grad_k, grad_v, moments = local
    returned_q = []
    returned_kv = []
    order = [2, 1] + list(range(3, GROUP_MOST))
    for hop in order:
        got, positional[hop], grad_q, grad_k, grad_v = lax.optimization_barrier(
            (arrived[hop], positional[hop], grad_q, grad_k, grad_v)
        )
        if hop in KEY_HOPS:
            terms = pair_terms(
                query_heads,
                grad_heads,
                log_block,
                delta_block,
                got[0],
                got[1],
                positional[hop],
                fire_w2,
            )
            grad_q = grad_q + terms[0]
            partial = jnp.stack([terms[1], terms[2]]).astype(jnp.bfloat16)
            returned_kv.append(sent_back(partial, "cp", hop))
        else:
            far_query, far_stats = got
            terms = pair_terms(
                far_query[0],
                far_query[1],
                far_stats[0],
                far_stats[1],
                key_heads,
                value_heads,
                positional[hop],
                fire_w2,
            )
            grad_k = grad_k + terms[1]
            grad_v = grad_v + terms[2]
            returned_q.append(sent_forward(terms[0].astype(jnp.bfloat16), "cp", hop))
        moments = moments + terms[3]
    for part in returned_q:
        grad_q = grad_q + part.astype(jnp.float32)
    for part in returned_kv:
        grad_k = grad_k + part[0].astype(jnp.float32)
        grad_v = grad_v + part[1].astype(jnp.float32)
    hid = fire_w1.shape[0]
    on_mask, on_ratio = moments[:hid], moments[hid:]
    first = jnp.sum(fire_w2 * on_ratio, axis=1)
    bias_sum = jnp.sum(fire_w2 * on_mask, axis=1)
    second = fire_w1[:, None] * on_ratio + fire_b1[:, None] * on_mask
    flat = jnp.concatenate([first, bias_sum, second.reshape(-1)])
    flat = radix_sum(flat, ("cp", "dp"))
    first, bias_sum, second = flat[:hid], flat[hid : 2 * hid], flat[2 * hid :].reshape(second.shape)
    factor = (lax.axis_size("dp") * cp_count * rows_dev) ** (-0.5)
    out_shape = (1, rows_dev, feature_count)
    return (
        grad_q.reshape(out_shape).astype(jnp.bfloat16),
        grad_k.reshape(out_shape).astype(jnp.bfloat16),
        grad_v.reshape(out_shape).astype(jnp.bfloat16),
        first * factor,
        bias_sum * factor,
        second * factor,
    )


def solution(mesh):
    placed = (
        P("dp", "cp", None),
        P("dp", "cp", None),
        P("dp", "cp", None),
        P("dp", "cp", None),
        P("dp", "cp", None),
        P("dp", "cp", None),
        P("dp", None),
        P(),
        P(),
        P(),
    )
    return jax.shard_map(
        on_device,
        mesh=mesh,
        in_specs=placed,
        out_specs=(P("dp", "cp", None), P("dp", "cp", None), P("dp", "cp", None), P(), P(), P()),
        check_vma=False,
    )
```

```python
import jax
import jax.numpy as jnp
from jax import lax
from jax.sharding import PartitionSpec as P

GROUP_MOST = 4

KEY_HOPS = ()


fire_floor = 64.0


def shifted_2(block, axis, distance):
    devices = range(lax.axis_size(axis))
    route = [(i - distance, i) for i in devices if i - distance in devices]
    return lax.ppermute(block, axis, route)


def shifted_3(shard, axis, by):
    count = lax.axis_size(axis)
    return lax.ppermute(shard, axis, [(i, (i + by) % count) for i in range(count)])


def seat_of(length_row, device):
    ends = jnp.cumsum(length_row)
    sequence = jnp.sum((ends <= device).astype(jnp.int32))
    before = jnp.sum(
        jnp.where(jnp.arange(length_row.shape[0], dtype=jnp.int32) < sequence, length_row, 0)
    )
    return (sequence, device - before)


def position_terms(query_seq, query_pos, key_seq, key_pos, fire_w1, fire_b1, fire_w2):
    allowed = (query_seq == key_seq) & (key_pos[None, :] <= query_pos[:, None])
    distance = jnp.maximum(query_pos[:, None] - key_pos[None, :], 0).astype(jnp.float32)
    denom = jnp.log1p(jnp.maximum(query_pos.astype(jnp.float32), fire_floor))
    ratio = jnp.log1p(distance) / denom[:, None]
    hidden_pre = fire_w1[:, None, None] * ratio[None] + fire_b1[:, None, None]
    hidden_act = jnp.maximum(hidden_pre, 0.0)
    pair_bias = jnp.einsum("cqk,ch->hqk", hidden_act, fire_w2, precision=lax.Precision.HIGH)
    live = (hidden_pre > 0).astype(jnp.float32)
    fire_basis = jnp.concatenate([live, live * ratio[None]], axis=0)
    return (allowed, pair_bias, fire_basis)


def pair_terms(
    query_heads,
    grad_heads,
    log_block,
    delta_block,
    key_heads,
    value_heads,
    positional,
    fire_w2,
):
    allowed, pair_bias, fire_basis = positional
    scale_value = query_heads.shape[2] ** (-0.5)
    scores = (
        jnp.einsum("hqd,hkd->hqk", query_heads, key_heads, preferred_element_type=jnp.float32)
        * scale_value
        + pair_bias
    )
    shifted = jnp.where(allowed[None], scores - log_block[:, :, None], -1e30)
    prob_block = jnp.exp(shifted)
    dprob = jnp.einsum("hqd,hkd->hqk", grad_heads, value_heads, preferred_element_type=jnp.float32)
    dscore = prob_block * (dprob - delta_block[:, :, None])
    prob_low = prob_block.astype(jnp.bfloat16)
    score_low = dscore.astype(jnp.bfloat16)
    grad_query = (
        jnp.einsum("hqk,hkd->hqd", score_low, key_heads, preferred_element_type=jnp.float32)
        * scale_value
    )
    grad_key = (
        jnp.einsum("hqk,hqd->hkd", score_low, query_heads, preferred_element_type=jnp.float32)
        * scale_value
    )
    grad_value = jnp.einsum(
        "hqk,hqd->hkd", prob_low, grad_heads, preferred_element_type=jnp.float32
    )
    moments = jnp.einsum("hqk,mqk->mh", dscore, fire_basis, precision=lax.Precision.HIGH)
    return (grad_query, grad_key, grad_value, moments)


def sent_back(block, axis, distance):
    count = lax.axis_size(axis)
    return lax.ppermute(block, axis, [(i, i - distance) for i in range(distance, count)])


def sent_forward(block, axis, distance):
    count = lax.axis_size(axis)
    return lax.ppermute(block, axis, [(i, i + distance) for i in range(count - distance)])


def radix_sum(block, axes):
    for axis in axes:
        count = lax.axis_size(axis)
        me = lax.axis_index(axis)
        stride = 1
        while stride < count:
            width = min(4, count // stride)
            digit = (me // stride) % width

            def moved(i, shift):
                d = (i // stride) % width
                return i + ((d + shift) % width - d) * stride

            got = [block] + [
                lax.ppermute(block, axis, [(i, moved(i, shift)) for i in range(count)])
                for shift in range(1, width)
            ]
            stacked = jnp.stack(got)
            ordered = [stacked[(digit - t) % width] for t in range(width)]
            total = ordered[0]
            for part in ordered[1:]:
                total = total + part
            block = total
            stride *= width
    return block


def on_device(queries, keys, values, outputs, d_out, log_norm, lengths, fire_w1, fire_b1, fire_w2):
    rows_dev = queries.shape[1]
    heads_count = log_norm.shape[2]
    feature_count = queries.shape[2]
    head_size = feature_count // heads_count
    cp_count = lax.axis_size("cp")
    my_index = lax.axis_index("cp")
    length_row = lengths[0]
    def head_major(block):
        return block[0].reshape(rows_dev, heads_count, head_size).transpose(1, 0, 2)

    query_heads = head_major(queries)
    key_heads = head_major(keys)
    value_heads = head_major(values)
    grad_heads = head_major(d_out)
    out_heads = head_major(outputs)
    log_block = log_norm[0].T
    delta_block = jnp.einsum(
        "hqd,hqd->hq", grad_heads, out_heads, preferred_element_type=jnp.float32
    )
    token_index = jnp.arange(rows_dev, dtype=jnp.int32)

    def seat_positions(device):
        sequence, offset = seat_of(length_row, device)
        return (sequence, offset * rows_dev + token_index)

    my_seq, my_pos = seat_positions(my_index)
    query_side = jnp.stack([query_heads, grad_heads])
    stats_side = jnp.stack([log_block, delta_block])
    key_side = jnp.stack([key_heads, value_heads])
    arrived = {}
    positional = {}
    for hop in range(1, GROUP_MOST):
        if hop in KEY_HOPS:
            arrived[hop] = sent_forward(key_side, "cp", hop)
            key_seq, key_pos = seat_positions((my_index - hop) % cp_count)
            key_seq = jnp.where(my_index >= hop, key_seq, -1)
            positional[hop] = position_terms(
                my_seq, my_pos, key_seq, key_pos, fire_w1, fire_b1, fire_w2
            )
        else:
            arrived[hop] = (sent_back(query_side, "cp", hop), sent_back(stats_side, "cp", hop))
            query_seq, query_pos = seat_positions(my_index + hop)
            query_seq = jnp.where(my_index + hop < cp_count, query_seq, -2)
            positional[hop] = position_terms(
                query_seq, query_pos, my_seq, my_pos, fire_w1, fire_b1, fire_w2
            )
    positional[0] = position_terms(my_seq, my_pos, my_seq, my_pos, fire_w1, fire_b1, fire_w2)
    local = pair_terms(
        query_heads,
        grad_heads,
        log_block,
        delta_block,
        key_heads,
        value_heads,
        positional[0],
        fire_w2,
    )
    grad_q, grad_k, grad_v, moments = local
    returned_q = []
    returned_kv = []
    order = [2, 1] + list(range(3, GROUP_MOST))
    for hop in order:
        got, positional[hop], grad_q, grad_k, grad_v = lax.optimization_barrier(
            (arrived[hop], positional[hop], grad_q, grad_k, grad_v)
        )
        if hop in KEY_HOPS:
            terms = pair_terms(
                query_heads,
                grad_heads,
                log_block,
                delta_block,
                got[0],
                got[1],
                positional[hop],
                fire_w2,
            )
            grad_q = grad_q + terms[0]
            partial = jnp.stack([terms[1], terms[2]]).astype(jnp.bfloat16)
            returned_kv.append(sent_back(partial, "cp", hop))
        else:
            far_query, far_stats = got
            terms = pair_terms(
                far_query[0],
                far_query[1],
                far_stats[0],
                far_stats[1],
                key_heads,
                value_heads,
                positional[hop],
                fire_w2,
            )
            grad_k = grad_k + terms[1]
            grad_v = grad_v + terms[2]
            returned_q.append(sent_forward(terms[0].astype(jnp.bfloat16), "cp", hop))
        moments = moments + terms[3]
    for part in returned_q:
        grad_q = grad_q + part.astype(jnp.float32)
    for part in returned_kv:
        grad_k = grad_k + part[0].astype(jnp.float32)
        grad_v = grad_v + part[1].astype(jnp.float32)
    hid = fire_w1.shape[0]
    on_mask, on_ratio = moments[:hid], moments[hid:]
    first = jnp.sum(fire_w2 * on_ratio, axis=1)
    bias_sum = jnp.sum(fire_w2 * on_mask, axis=1)
    second = fire_w1[:, None] * on_ratio + fire_b1[:, None] * on_mask
    flat = jnp.concatenate([first, bias_sum, second.reshape(-1)])
    flat = radix_sum(flat, ("cp", "dp"))
    first, bias_sum, second = flat[:hid], flat[hid : 2 * hid], flat[2 * hid :].reshape(second.shape)
    factor = (lax.axis_size("dp") * cp_count * rows_dev) ** (-0.5)
    out_shape = (1, rows_dev, feature_count)

    def token_major(block):
        return block.astype(jnp.bfloat16).transpose(1, 0, 2).reshape(out_shape)

    return (
        token_major(grad_q),
        token_major(grad_k),
        token_major(grad_v),
        first * factor,
        bias_sum * factor,
        second * factor,
    )


def solution(mesh):
    placed = (
        P("dp", "cp", None),
        P("dp", "cp", None),
        P("dp", "cp", None),
        P("dp", "cp", None),
        P("dp", "cp", None),
        P("dp", "cp", None),
        P("dp", None),
        P(),
        P(),
        P(),
    )
    return jax.shard_map(
        on_device,
        mesh=mesh,
        in_specs=placed,
        out_specs=(P("dp", "cp", None), P("dp", "cp", None), P("dp", "cp", None), P(), P(), P()),
        check_vma=False,
    )
```
